32 devices in a mesh: row: 16 (over z, x, core), col: 2 (over y).
Axes of the slice: x: 2, y: 2, z: 4, core: 2. Of those that a mesh axis runs over, the one named last changes fastest.
Arguments:
- counts: int32 [3072, 3072], P('row', 'col'), may hold values from 0 to 3
- theta: bfloat16 [3072, 64], P(('row', 'col')), may hold values from 0.099609375 to 1
- phi: bfloat16 [3072, 64], P(('col', 'row')), may hold values from 0.099609375 to 1
- affinity: float32 [64, 64], replicated, may hold values from 0.0003 to 0.003
Outputs:
- theta_grad: float32 [3072, 64], P(('row', 'col'))
- phi_grad: float32 [3072, 64], P(('col', 'row'))
- affinity_grad: float32 [64, 64], replicated
The draws below stay inside these ranges and needn't reach their ends.
All inputs are finite; a program needn't handle non-finite values.
Results may differ from the reference program's by a relative error of at most 0.0003.
Values may be sent and summed in bfloat16 or wider, within the bound.
No kernel may reach another device: no remote copies, remote signals or barrier semaphores. Data moves between devices by JAX's collectives and lax.ppermute only.
A program may use at most 64 MiB of HBM per device.

```python
import math
import jax
import jax.numpy as jnp
from jax import lax

K = 64
NODES = 3072


def plant(values, stream_key, low, high):
    longest = values.shape.index(max(values.shape))
    spots = []
    for shift in (0, 1):
        where = [jax.random.randint(jax.random.fold_in(stream_key, axis), (), 0, length) for axis, length in enumerate(values.shape)]
        where[longest] = (where[longest] + shift) % values.shape[longest]
        spots.append(tuple(where))
    return values.at[spots[0]].set(low).at[spots[1]].set(high)


def block_levels(rng, extent, split, least, top_value):
    factor_of, own = 1.0, jax.random.fold_in(rng, 6)
    for position, blocks in split:
        steps = jnp.exp(jax.random.uniform(jax.random.fold_in(own, position), (blocks,), jnp.float32, least / len(split), top_value / len(split)))
        factor_of = factor_of * jnp.repeat(steps, extent[position] // blocks).reshape([-1 if axis == position else 1 for axis in range(len(extent))])
    return factor_of


def setup_inputs(seed: int = 0) -> dict:
    key_of = jax.random.split(jax.random.key(seed), 5)
    return {
        "counts": plant(jax.random.randint(key_of[0], (NODES, NODES), 0, 4), jax.random.fold_in(key_of[0], 1), 0, 3).astype(jnp.int32),
        "theta": jnp.clip(jnp.exp(math.log(1.0) - 2.306499 * jax.random.uniform(key_of[1], (NODES, K), jnp.float32) ** block_levels(key_of[1], (NODES, K), ((0, 32),), -0.2, 0.2)), 0.099609375, 1.0).astype(jnp.bfloat16),
        "phi": jnp.clip(jnp.exp(math.log(1.0) - 2.306499 * jax.random.uniform(key_of[2], (NODES, K), jnp.float32) ** block_levels(key_of[2], (NODES, K), ((0, 32),), -0.2, 0.2)), 0.099609375, 1.0).astype(jnp.bfloat16),
        "affinity": jnp.clip(jnp.exp(jax.random.uniform(key_of[3], (K, K), jnp.float32, math.log(0.0003), math.log(0.003))), 0.0003, 0.003),
    }


def reference(counts, theta, phi, affinity):
    nodes = counts.shape[0]
    inverse = 1.0 / nodes
    width = affinity.shape[0]
    row_factor = jnp.dot(theta.astype(jnp.float32), affinity, precision=lax.Precision.HIGHEST)
    factor_half = row_factor.astype(jnp.bfloat16)
    phi_wide = phi.astype(jnp.float32)
    count_blocks = counts.reshape(16, nodes // 16, nodes)
    factor_blocks = row_factor.reshape(16, nodes // 16, width)
    half_blocks = factor_half.reshape(16, nodes // 16, width)

    def one_block(gcol, blocks):
        count_rows, factor_rows, half_rows = blocks
        rate = jnp.dot(factor_rows, phi_wide.T, precision=lax.Precision.HIGHEST)
        ratio = (1.0 - count_rows.astype(jnp.float32) / rate).astype(jnp.bfloat16)
        gphi_rows = jnp.dot(ratio, phi, preferred_element_type=jnp.float32)
        gcol = gcol + jnp.dot(ratio.T, half_rows, preferred_element_type=jnp.float32)
        return gcol, gphi_rows

    start = jnp.zeros((nodes, width), jnp.float32)
    gcol, gphi_blocks = lax.scan(one_block, start, (count_blocks, factor_blocks, half_blocks))
    gphi = gphi_blocks.reshape(nodes, width)
    theta_grad = inverse * jnp.dot(gphi, affinity.T, precision=lax.Precision.HIGHEST)
    phi_grad = inverse * gcol
    affinity_grad = inverse * inverse * jnp.dot(theta.astype(jnp.float32).T, gphi, precision=lax.Precision.HIGHEST)
    return theta_grad, phi_grad, affinity_grad
```

```python
import jax
import jax.numpy as jnp
from jax import lax
from jax.sharding import PartitionSpec as P

HI = lax.Precision.HIGHEST


def gather_rows(x, axis):
    n = lax.axis_size(axis)
    slots = jnp.broadcast_to(x[None], (n,) + x.shape)
    got = lax.all_to_all(slots, axis, 0, 0)
    return got.reshape((n * x.shape[0],) + x.shape[1:])


def shards(counts, theta, phi, affinity):
    nr, nc = lax.axis_size("row"), lax.axis_size("col")
    nodes = theta.shape[0] * nr * nc
    inverse = 1.0 / nodes
    k = theta.shape[1]
    c = lax.axis_index("col")
    if nc == 2:
        other = lax.ppermute(theta, "col", [(0, 1), (1, 0)])
        theta_rows = jnp.where(c == 0, jnp.concatenate([theta, other]), jnp.concatenate([other, theta]))
    else:
        theta_rows = gather_rows(theta, "col")
    members = gather_rows(phi, "row")
    theta_wide = theta_rows.astype(jnp.float32)
    row_factor = jnp.dot(theta_wide, affinity, precision=HI)
    factor_half = row_factor.astype(jnp.bfloat16)
    rate = jnp.dot(row_factor, members.astype(jnp.float32).T, precision=HI)
    ratio = (1.0 - counts.astype(jnp.float32) / rate).astype(jnp.bfloat16)
    gphi = jnp.dot(ratio, members, preferred_element_type=jnp.float32)
    gcol = lax.dot_general(ratio, factor_half, (((0,), (0,)), ((), ())), preferred_element_type=jnp.float32)
    part = jnp.dot(theta_wide.T, gphi, precision=HI)
    mc = gphi.shape[0] // nc
    if nc == 2:
        send = jnp.concatenate([lax.dynamic_slice_in_dim(gphi, (1 - c) * mc, mc), part])
        got = lax.ppermute(send, "col", [(0, 1), (1, 0)])
        gphi_sum = lax.dynamic_slice_in_dim(gphi, c * mc, mc) + got[:mc]
        part_col = part + got[mc:]
    else:
        slots = jnp.concatenate([gphi.reshape(nc, mc, k), jnp.broadcast_to(part[None], (nc, k, k))], axis=1)
        got = lax.all_to_all(slots, "col", 0, 0)
        gphi_sum = jnp.sum(got[:, :mc], axis=0)
        part_col = jnp.sum(got[:, mc:], axis=0)
    mr = gcol.shape[0] // nr
    slots = jnp.concatenate([gcol.reshape(nr, mr, k), jnp.broadcast_to(part_col[None], (nr, k, k))], axis=1)
    got = lax.all_to_all(slots, "row", 0, 0)
    phi_sum = jnp.sum(got[:, :mr], axis=0)
    part_all = jnp.sum(got[:, mr:], axis=0)
    theta_grad = inverse * jnp.dot(gphi_sum, affinity.T, precision=HI)
    phi_grad = inverse * phi_sum
    affinity_grad = inverse * inverse * part_all
    return (theta_grad, phi_grad, affinity_grad)


def solution(mesh):
    placed = (P("row", "col"), P(("row", "col"), None), P(("col", "row"), None), P())
    return jax.shard_map(
        shards,
        mesh=mesh,
        in_specs=placed,
        out_specs=(P(("row", "col"), None), P(("col", "row"), None), P()),
        check_vma=False,
    )
```

```python
import jax
import jax.numpy as jnp
from jax import lax
from jax.sharding import PartitionSpec as P

HI = lax.Precision.HIGHEST


def gather_rows(x, axis):
    n = lax.axis_size(axis)
    slots = jnp.broadcast_to(x[None], (n,) + x.shape)
    got = lax.all_to_all(slots, axis, 0, 0)
    return got.reshape((n * x.shape[0],) + x.shape[1:])


def shards(counts, theta, phi, affinity):
    nr, nc = lax.axis_size("row"), lax.axis_size("col")
    nodes = theta.shape[0] * nr * nc
    inverse = 1.0 / nodes
    k = theta.shape[1]
    c = lax.axis_index("col")
    if nc == 2:
        other = lax.ppermute(theta, "col", [(0, 1), (1, 0)])
        theta_rows = jnp.where(c == 0, jnp.concatenate([theta, other]), jnp.concatenate([other, theta]))
    else:
        theta_rows = gather_rows(theta, "col")
    members = gather_rows(phi, "row")
    theta_wide = theta_rows.astype(jnp.float32)
    row_factor = jnp.dot(theta_wide, affinity, precision=HI)
    factor_half = row_factor.astype(jnp.bfloat16)
    rate = jnp.dot(row_factor, members.astype(jnp.float32).T, precision=HI)
    ratio = (1.0 - counts.astype(jnp.float32) / rate).astype(jnp.bfloat16)
    gphi = jnp.dot(ratio, members, preferred_element_type=jnp.float32)
    gcol = lax.dot_general(ratio, factor_half, (((0,), (0,)), ((), ())), preferred_element_type=jnp.float32)
    part = jnp.dot(theta_wide.T, gphi, precision=HI)
    mc = gphi.shape[0] // nc
    if nc == 2:
        send = jnp.concatenate([lax.dynamic_slice_in_dim(gphi, (1 - c) * mc, mc), part])
        got = lax.ppermute(send, "col", [(0, 1), (1, 0)])
        gphi_sum = lax.dynamic_slice_in_dim(gphi, c * mc, mc) + got[:mc]
        part_col = part + got[mc:]
    else:
        slots = jnp.concatenate([gphi.reshape(nc, mc, k), jnp.broadcast_to(part[None], (nc, k, k))], axis=1)
        got = lax.all_to_all(slots, "col", 0, 0)
        gphi_sum = jnp.sum(got[:, :mc], axis=0)
        part_col = jnp.sum(got[:, mc:], axis=0)
    mr = gcol.shape[0] // nr
    got = lax.all_to_all(gcol.reshape(nr, mr, k), "row", 0, 0)
    phi_sum = jnp.sum(got, axis=0)
    part_all = part_col
    step = 1
    while step < nr:
        part_all = part_all + lax.ppermute(part_all, "row", [(i, i ^ step) for i in range(nr)])
        step *= 2
    theta_grad = inverse * jnp.dot(gphi_sum, affinity.T, precision=HI)
    phi_grad = inverse * phi_sum
    affinity_grad = inverse * inverse * part_all
    return (theta_grad, phi_grad, affinity_grad)


def solution(mesh):
    placed = (P("row", "col"), P(("row", "col"), None), P(("col", "row"), None), P())
    return jax.shard_map(
        shards,
        mesh=mesh,
        in_specs=placed,
        out_specs=(P(("row", "col"), None), P(("col", "row"), None), P()),
        check_vma=False,
    )
```

```python
import jax
import jax.numpy as jnp
from jax import lax
from jax.sharding import Mesh, PartitionSpec as P

HI = lax.Precision.HIGHEST
SWAP = [(0, 1), (1, 0)]
ROW = ("chip", "core")
TREE_GATHER = False


def gather_rows(x, axis):
    n = lax.axis_size(axis)
    slots = jnp.broadcast_to(x[None], (n,) + x.shape)
    got = lax.all_to_all(slots, axis, 0, 0)
    return got.reshape((n * x.shape[0],) + x.shape[1:])


def tree_gather(x, axis):
    n = lax.axis_size(axis)
    me = lax.axis_index(axis)
    bits = []
    b = n // 2
    while b >= 1:
        bits.append(b)
        b //= 2
    held = x[None]
    for b in bits:
        held = jnp.concatenate([held, lax.ppermute(held, axis, [(i, i ^ b) for i in range(n)])])
    rel = me ^ jnp.arange(n)
    slot = sum(((rel // b) % 2) << j for j, b in enumerate(bits))
    return jnp.take(held, slot, axis=0).reshape((n * x.shape[0],) + x.shape[1:])


def shards(counts, theta, phi, affinity):
    nr, nc = lax.axis_size(ROW), lax.axis_size("col")
    assert nr & (nr - 1) == 0
    nodes = theta.shape[0] * nr * nc
    inverse = 1.0 / nodes
    k = theta.shape[1]
    c = lax.axis_index("col")
    r = lax.axis_index(ROW)
    if nc == 2:
        other = lax.ppermute(theta, "col", SWAP)
        theta_rows = jnp.where(c == 0, jnp.concatenate([theta, other]), jnp.concatenate([other, theta]))
    else:
        theta_rows = gather_rows(theta, "col")
    nchip = lax.axis_size("chip")
    core = lax.axis_index("core")
    by_chip = lax.all_to_all(jnp.broadcast_to(phi[None], (nchip,) + phi.shape), "chip", 0, 0)
    other = lax.ppermute(by_chip, "core", SWAP)
    pair = jnp.where(core == 0, jnp.stack([by_chip, other], axis=1), jnp.stack([other, by_chip], axis=1))
    members = pair.reshape(nr * phi.shape[0], k)
    theta_wide = theta_rows.astype(jnp.float32)
    row_factor = jnp.dot(theta_wide, affinity, precision=HI)
    factor_half = row_factor.astype(jnp.bfloat16)
    rate = jnp.dot(row_factor, members.astype(jnp.float32).T, precision=HI)
    ratio = (1.0 - counts.astype(jnp.float32) / rate).astype(jnp.bfloat16)
    gphi = jnp.dot(ratio, members, preferred_element_type=jnp.float32)
    gcol = lax.dot_general(ratio, factor_half, (((0,), (0,)), ((), ())), preferred_element_type=jnp.float32)
    part = jnp.dot(theta_wide.T, gphi, precision=HI)
    mc = gphi.shape[0] // nc
    if nc == 2:
        send = jnp.concatenate([lax.dynamic_slice_in_dim(gphi, (1 - c) * mc, mc), part])
        got = lax.ppermute(send, "col", SWAP)
        gphi_sum = lax.dynamic_slice_in_dim(gphi, c * mc, mc) + got[:mc]
        part_sum = part + got[mc:]
    else:
        slots = jnp.concatenate([gphi.reshape(nc, mc, k), jnp.broadcast_to(part[None], (nc, k, k))], axis=1)
        got = lax.all_to_all(slots, "col", 0, 0)
        gphi_sum = jnp.sum(got[:, :mc], axis=0)
        part_sum = jnp.sum(got[:, mc:], axis=0)
    mr = gcol.shape[0] // nr
    acc = gcol.reshape(nr, mr, k)
    b = 1
    while b < nr:
        pairs = acc.reshape(acc.shape[0] // 2, 2, mr, k)
        mine = (r // b) % 2
        keep = jnp.take(pairs, mine, axis=1)
        away = jnp.take(pairs, 1 - mine, axis=1)
        send = jnp.concatenate([away.reshape(-1, k), part_sum])
        got = lax.ppermute(send, ROW, [(i, i ^ b) for i in range(nr)])
        acc = keep + got[: keep.shape[0] * mr].reshape(keep.shape)
        part_sum = part_sum + got[keep.shape[0] * mr:]
        b *= 2
    phi_sum = acc[0]
    theta_grad = inverse * jnp.dot(gphi_sum, affinity.T, precision=HI)
    phi_grad = inverse * phi_sum
    affinity_grad = inverse * inverse * part_sum
    return (theta_grad, phi_grad, affinity_grad)


def solution(mesh):
    rows, cols = mesh.devices.shape
    split = Mesh(mesh.devices.reshape(rows // 2, 2, cols), ("chip", "core", "col"))
    placed = (P(ROW, "col"), P(ROW + ("col",), None), P(("col",) + ROW, None), P())
    return jax.shard_map(
        shards,
        mesh=split,
        in_specs=placed,
        out_specs=(P(ROW + ("col",), None), P(("col",) + ROW, None), P()),
        check_vma=False,
    )
```

```python
import jax
import jax.numpy as jnp
from jax import lax
from jax.sharding import Mesh, PartitionSpec as P

HI = lax.Precision.HIGHEST
SWAP = [(0, 1), (1, 0)]
ROW = ("chip", "core")
TREE_GATHER = False


def gather_rows(x, axis):
    n = lax.axis_size(axis)
    slots = jnp.broadcast_to(x[None], (n,) + x.shape)
    got = lax.all_to_all(slots, axis, 0, 0)
    return got.reshape((n * x.shape[0],) + x.shape[1:])


def tree_gather(x, axis):
    n = lax.axis_size(axis)
    me = lax.axis_index(axis)
    bits = []
    b = n // 2
    while b >= 1:
        bits.append(b)
        b //= 2
    held = x[None]
    for b in bits:
        held = jnp.concatenate([held, lax.ppermute(held, axis, [(i, i ^ b) for i in range(n)])])
    rel = me ^ jnp.arange(n)
    slot = sum(((rel // b) % 2) << j for j, b in enumerate(bits))
    return jnp.take(held, slot, axis=0).reshape((n * x.shape[0],) + x.shape[1:])


def shards(counts, theta, phi, affinity):
    nr, nc = lax.axis_size(ROW), lax.axis_size("col")
    assert nr & (nr - 1) == 0
    nodes = theta.shape[0] * nr * nc
    inverse = 1.0 / nodes
    k = theta.shape[1]
    c = lax.axis_index("col")
    r = lax.axis_index(ROW)
    if nc == 2:
        other = lax.ppermute(theta, "col", SWAP)
        theta_rows = jnp.where(c == 0, jnp.concatenate([theta, other]), jnp.concatenate([other, theta]))
    else:
        theta_rows = gather_rows(theta, "col")
    nchip = lax.axis_size("chip")
    core = lax.axis_index("core")
    by_chip = lax.all_to_all(jnp.broadcast_to(phi[None], (nchip,) + phi.shape), "chip", 0, 0)
    other = lax.ppermute(by_chip, "core", SWAP)
    pair = jnp.where(core == 0, jnp.stack([by_chip, other], axis=1), jnp.stack([other, by_chip], axis=1))
    members = pair.reshape(nr * phi.shape[0], k)
    theta_wide = theta_rows.astype(jnp.float32)
    row_factor = jnp.dot(theta_wide, affinity, precision=HI)
    factor_half = row_factor.astype(jnp.bfloat16)
    rate = jnp.dot(row_factor, members.astype(jnp.float32).T, precision=HI)
    ratio = (1.0 - counts.astype(jnp.float32) / rate).astype(jnp.bfloat16)
    gphi = jnp.dot(ratio, members, preferred_element_type=jnp.float32)
    gcol = lax.dot_general(ratio, factor_half, (((0,), (0,)), ((), ())), preferred_element_type=jnp.float32)
    part = jnp.dot(theta_wide.T, gphi, precision=HI)
    mc = gphi.shape[0] // nc
    if nc == 2:
        send = jnp.concatenate([lax.dynamic_slice_in_dim(gphi, (1 - c) * mc, mc), part])
        got = lax.ppermute(send, "col", SWAP)
        gphi_sum = lax.dynamic_slice_in_dim(gphi, c * mc, mc) + got[:mc]
        part_sum = part + got[mc:]
    else:
        slots = jnp.concatenate([gphi.reshape(nc, mc, k), jnp.broadcast_to(part[None], (nc, k, k))], axis=1)
        got = lax.all_to_all(slots, "col", 0, 0)
        gphi_sum = jnp.sum(got[:, :mc], axis=0)
        part_sum = jnp.sum(got[:, mc:], axis=0)
    mr = gcol.shape[0] // nr
    acc = gcol.reshape(nr, mr, k)
    b = 1
    while b < nr // 4:
        pairs = acc.reshape(acc.shape[0] // 2, 2, mr, k)
        mine = (r // b) % 2
        keep = jnp.take(pairs, mine, axis=1)
        away = jnp.take(pairs, 1 - mine, axis=1)
        send = jnp.concatenate([away.reshape(-1, k), part_sum])
        got = lax.ppermute(send, ROW, [(i, i ^ b) for i in range(nr)])
        acc = keep + got[: keep.shape[0] * mr].reshape(keep.shape)
        part_sum = part_sum + got[keep.shape[0] * mr:]
        b *= 2
    if acc.shape[0] == 4:
        quad = (r // b) % 4
        held = [part_sum]
        total = jnp.take(acc, quad, axis=0)
        for s in (1, 2, 3):
            send = jnp.concatenate([jnp.take(acc, quad ^ s, axis=0), part_sum])
            got = lax.ppermute(send, ROW, [(i, i ^ (s * b)) for i in range(nr)])
            total = total + got[:mr]
            held.append(got[mr:])
        part_sum = jnp.sum(jnp.take(jnp.stack(held), quad ^ jnp.arange(4), axis=0), axis=0)
        acc = total[None]
    elif acc.shape[0] == 2:
        mine = (r // b) % 2
        send = jnp.concatenate([jnp.take(acc, 1 - mine, axis=0), part_sum])
        got = lax.ppermute(send, ROW, [(i, i ^ b) for i in range(nr)])
        acc = (jnp.take(acc, mine, axis=0) + got[:mr])[None]
        part_sum = part_sum + got[mr:]
    phi_sum = acc[0]
    theta_grad = inverse * jnp.dot(gphi_sum, affinity.T, precision=HI)
    phi_grad = inverse * phi_sum
    affinity_grad = inverse * inverse * part_sum
    return (theta_grad, phi_grad, affinity_grad)


def solution(mesh):
    rows, cols = mesh.devices.shape
    split = Mesh(mesh.devices.reshape(rows // 2, 2, cols), ("chip", "core", "col"))
    placed = (P(ROW, "col"), P(ROW + ("col",), None), P(("col",) + ROW, None), P())
    return jax.shard_map(
        shards,
        mesh=split,
        in_specs=placed,
        out_specs=(P(ROW + ("col",), None), P(("col",) + ROW, None), P()),
        check_vma=False,
    )
```

```python
import jax
import jax.numpy as jnp
from jax import lax
from jax.sharding import Mesh, PartitionSpec as P

HI = lax.Precision.HIGHEST
SWAP = [(0, 1), (1, 0)]
ROW = ("chip", "core")
TREE_GATHER = False


def gather_rows(x, axis):
    n = lax.axis_size(axis)
    slots = jnp.broadcast_to(x[None], (n,) + x.shape)
    got = lax.all_to_all(slots, axis, 0, 0)
    return got.reshape((n * x.shape[0],) + x.shape[1:])


def tree_gather(x, axis):
    n = lax.axis_size(axis)
    me = lax.axis_index(axis)
    bits = []
    b = n // 2
    while b >= 1:
        bits.append(b)
        b //= 2
    held = x[None]
    for b in bits:
        held = jnp.concatenate([held, lax.ppermute(held, axis, [(i, i ^ b) for i in range(n)])])
    rel = me ^ jnp.arange(n)
    slot = sum(((rel // b) % 2) << j for j, b in enumerate(bits))
    return jnp.take(held, slot, axis=0).reshape((n * x.shape[0],) + x.shape[1:])


def shards(counts, theta, phi, affinity):
    nr, nc = lax.axis_size(ROW), lax.axis_size("col")
    assert nr & (nr - 1) == 0
    nodes = theta.shape[0] * nr * nc
    inverse = 1.0 / nodes
    k = theta.shape[1]
    c = lax.axis_index("col")
    r = lax.axis_index(ROW)
    if nc == 2:
        other = lax.ppermute(theta, "col", SWAP)
        theta_rows = jnp.where(c == 0, jnp.concatenate([theta, other]), jnp.concatenate([other, theta]))
    else:
        theta_rows = gather_rows(theta, "col")
    nchip = lax.axis_size("chip")
    core = lax.axis_index("core")
    by_chip = lax.all_to_all(jnp.broadcast_to(phi[None], (nchip,) + phi.shape), "chip", 0, 0)
    other = lax.ppermute(by_chip, "core", SWAP)
    pair = jnp.where(core == 0, jnp.stack([by_chip, other], axis=1), jnp.stack([other, by_chip], axis=1))
    members = pair.reshape(nr * phi.shape[0], k)
    theta_wide = theta_rows.astype(jnp.float32)
    row_factor = jnp.dot(theta_wide, affinity, precision=HI)
    factor_half = row_factor.astype(jnp.bfloat16)
    rate = jnp.dot(row_factor, members.astype(jnp.float32).T, precision=HI)
    ratio = (1.0 - counts.astype(jnp.float32) / rate).astype(jnp.bfloat16)
    gphi = jnp.dot(ratio, members, preferred_element_type=jnp.float32)
    gcol = lax.dot_general(ratio, factor_half, (((0,), (0,)), ((), ())), preferred_element_type=jnp.float32)
    part = lax.dot_general(gphi, theta_wide, (((0,), (0,)), ((), ())), precision=HI)
    mc = gphi.shape[0] // nc
    if nc == 2:
        send = jnp.concatenate([lax.dynamic_slice_in_dim(gphi, (1 - c) * mc, mc), part])
        got = lax.ppermute(send, "col", SWAP)
        gphi_sum = lax.dynamic_slice_in_dim(gphi, c * mc, mc) + got[:mc]
        part_sum = part + got[mc:]
    else:
        slots = jnp.concatenate([gphi.reshape(nc, mc, k), jnp.broadcast_to(part[None], (nc, k, k))], axis=1)
        got = lax.all_to_all(slots, "col", 0, 0)
        gphi_sum = jnp.sum(got[:, :mc], axis=0)
        part_sum = jnp.sum(got[:, mc:], axis=0)
    mr = gcol.shape[0] // nr
    acc = gcol.reshape(nr, mr, k)
    b = 1
    while b < nr // 4:
        pairs = acc.reshape(acc.shape[0] // 2, 2, mr, k)
        mine = (r // b) % 2
        keep = jnp.take(pairs, mine, axis=1)
        away = jnp.take(pairs, 1 - mine, axis=1)
        send = jnp.concatenate([away.reshape(-1, k), part_sum])
        got = lax.ppermute(send, ROW, [(i, i ^ b) for i in range(nr)])
        acc = keep + got[: keep.shape[0] * mr].reshape(keep.shape)
        part_sum = part_sum + got[keep.shape[0] * mr:]
        b *= 2
    if acc.shape[0] == 4:
        quad = (r // b) % 4
        held = [part_sum]
        total = jnp.take(acc, quad, axis=0)
        for s in (1, 2, 3):
            send = jnp.concatenate([jnp.take(acc, quad ^ s, axis=0), part_sum])
            got = lax.ppermute(send, ROW, [(i, i ^ (s * b)) for i in range(nr)])
            total = total + got[:mr]
            held.append(got[mr:])
        part_sum = (held[0] + held[1]) + (held[2] + held[3])
        acc = total[None]
    elif acc.shape[0] == 2:
        mine = (r // b) % 2
        send = jnp.concatenate([jnp.take(acc, 1 - mine, axis=0), part_sum])
        got = lax.ppermute(send, ROW, [(i, i ^ b) for i in range(nr)])
        acc = (jnp.take(acc, mine, axis=0) + got[:mr])[None]
        part_sum = part_sum + got[mr:]
    phi_sum = acc[0]
    theta_grad = inverse * jnp.dot(gphi_sum, affinity.T, precision=HI)
    phi_grad = inverse * phi_sum
    affinity_grad = inverse * inverse * part_sum.T
    return (theta_grad, phi_grad, affinity_grad)


def solution(mesh):
    rows, cols = mesh.devices.shape
    split = Mesh(mesh.devices.reshape(rows // 2, 2, cols), ("chip", "core", "col"))
    placed = (P(ROW, "col"), P(ROW + ("col",), None), P(("col",) + ROW, None), P())
    return jax.shard_map(
        shards,
        mesh=split,
        in_specs=placed,
        out_specs=(P(ROW + ("col",), None), P(("col",) + ROW, None), P()),
        check_vma=False,
    )
```

```python
import jax
import jax.numpy as jnp
from jax import lax
from jax.sharding import Mesh, PartitionSpec as P

HI = lax.Precision.HIGHEST
SWAP = [(0, 1), (1, 0)]
ROW = ("chip", "core")
TREE_GATHER = False


def gather_rows(x, axis):
    n = lax.axis_size(axis)
    slots = jnp.broadcast_to(x[None], (n,) + x.shape)
    got = lax.all_to_all(slots, axis, 0, 0)
    return got.reshape((n * x.shape[0],) + x.shape[1:])


def tree_gather(x, axis):
    n = lax.axis_size(axis)
    me = lax.axis_index(axis)
    bits = []
    b = n // 2
    while b >= 1:
        bits.append(b)
        b //= 2
    held = x[None]
    for b in bits:
        held = jnp.concatenate([held, lax.ppermute(held, axis, [(i, i ^ b) for i in range(n)])])
    rel = me ^ jnp.arange(n)
    slot = sum(((rel // b) % 2) << j for j, b in enumerate(bits))
    return jnp.take(held, slot, axis=0).reshape((n * x.shape[0],) + x.shape[1:])


def shards(counts, theta, phi, affinity):
    nr, nc = lax.axis_size(ROW), lax.axis_size("col")
    assert nr & (nr - 1) == 0
    nodes = theta.shape[0] * nr * nc
    inverse = 1.0 / nodes
    k = theta.shape[1]
    c = lax.axis_index("col")
    r = lax.axis_index(ROW)
    if nc == 2:
        other = lax.ppermute(theta, "col", SWAP)
        theta_rows = jnp.where(c == 0, jnp.concatenate([theta, other]), jnp.concatenate([other, theta]))
    else:
        theta_rows = gather_rows(theta, "col")
    nchip = lax.axis_size("chip")
    core = lax.axis_index("core")
    by_chip = lax.all_to_all(jnp.broadcast_to(phi[None], (nchip,) + phi.shape), "chip", 0, 0)
    other = lax.ppermute(by_chip, "core", SWAP)
    pair = jnp.where(core == 0, jnp.stack([by_chip, other], axis=1), jnp.stack([other, by_chip], axis=1))
    members = pair.reshape(nr * phi.shape[0], k)
    theta_wide = theta_rows.astype(jnp.float32)
    row_factor = jnp.dot(theta_wide, affinity, precision=HI)
    factor_half = row_factor.astype(jnp.bfloat16)
    rate = jnp.dot(row_factor, members.astype(jnp.float32).T, precision=HI)
    ratio = (1.0 - counts.astype(jnp.float32) / rate).astype(jnp.bfloat16)
    gphi = jnp.dot(ratio, members, preferred_element_type=jnp.float32)
    gcol = lax.dot_general(ratio, factor_half, (((0,), (0,)), ((), ())), preferred_element_type=jnp.float32)
    part = lax.dot_general(gphi, theta_wide, (((0,), (0,)), ((), ())), precision=HI)
    mc = gphi.shape[0] // nc
    deferred = nc == 2 and nr >= 8
    if deferred:
        part_sum = part
    elif nc == 2:
        send = jnp.concatenate([lax.dynamic_slice_in_dim(gphi, (1 - c) * mc, mc), part])
        got = lax.ppermute(send, "col", SWAP)
        gphi_sum = lax.dynamic_slice_in_dim(gphi, c * mc, mc) + got[:mc]
        part_sum = part + got[mc:]
    else:
        slots = jnp.concatenate([gphi.reshape(nc, mc, k), jnp.broadcast_to(part[None], (nc, k, k))], axis=1)
        got = lax.all_to_all(slots, "col", 0, 0)
        gphi_sum = jnp.sum(got[:, :mc], axis=0)
        part_sum = jnp.sum(got[:, mc:], axis=0)
    mr = gcol.shape[0] // nr
    acc = gcol.reshape(nr, mr, k)
    b = 1
    while b < nr // 4:
        pairs = acc.reshape(acc.shape[0] // 2, 2, mr, k)
        mine = (r // b) % 2
        keep = jnp.take(pairs, mine, axis=1)
        away = jnp.take(pairs, 1 - mine, axis=1)
        send = jnp.concatenate([away.reshape(-1, k), part_sum])
        got = lax.ppermute(send, ROW, [(i, i ^ b) for i in range(nr)])
        acc = keep + got[: keep.shape[0] * mr].reshape(keep.shape)
        if deferred and b == 2:
            send = jnp.concatenate([lax.dynamic_slice_in_dim(gphi, (1 - c) * mc, mc), part_sum])
            got_col = lax.ppermute(send, "col", SWAP)
            got_diag = lax.ppermute(part_sum, ROW + ("col",), [(i, i ^ (2 * b + 1)) for i in range(nr * nc)])
            gphi_sum = lax.dynamic_slice_in_dim(gphi, c * mc, mc) + got_col[:mc]
            part_sum = (part_sum + got_col[mc:]) + (got[keep.shape[0] * mr:] + got_diag)
            deferred = False
        else:
            part_sum = part_sum + got[keep.shape[0] * mr:]
        b *= 2
    if acc.shape[0] == 4:
        quad = (r // b) % 4
        held = [part_sum]
        total = jnp.take(acc, quad, axis=0)
        for s in (1, 2, 3):
            send = jnp.concatenate([jnp.take(acc, quad ^ s, axis=0), part_sum])
            got = lax.ppermute(send, ROW, [(i, i ^ (s * b)) for i in range(nr)])
            total = total + got[:mr]
            held.append(got[mr:])
        part_sum = (held[0] + held[1]) + (held[2] + held[3])
        acc = total[None]
    elif acc.shape[0] == 2:
        mine = (r // b) % 2
        send = jnp.concatenate([jnp.take(acc, 1 - mine, axis=0), part_sum])
        got = lax.ppermute(send, ROW, [(i, i ^ b) for i in range(nr)])
        acc = (jnp.take(acc, mine, axis=0) + got[:mr])[None]
        part_sum = part_sum + got[mr:]
    phi_sum = acc[0]
    theta_grad = inverse * jnp.dot(gphi_sum, affinity.T, precision=HI)
    phi_grad = inverse * phi_sum
    affinity_grad = inverse * inverse * part_sum.T
    return (theta_grad, phi_grad, affinity_grad)


def solution(mesh):
    rows, cols = mesh.devices.shape
    split = Mesh(mesh.devices.reshape(rows // 2, 2, cols), ("chip", "core", "col"))
    placed = (P(ROW, "col"), P(ROW + ("col",), None), P(("col",) + ROW, None), P())
    return jax.shard_map(
        shards,
        mesh=split,
        in_specs=placed,
        out_specs=(P(ROW + ("col",), None), P(("col",) + ROW, None), P()),
        check_vma=False,
    )
```

```python
import jax
import jax.numpy as jnp
from jax import lax
from jax.sharding import Mesh, PartitionSpec as P

HI = lax.Precision.HIGHEST
SWAP = [(0, 1), (1, 0)]
ROW = ("chip", "core")
TREE_GATHER = False


def gather_rows(x, axis):
    n = lax.axis_size(axis)
    slots = jnp.broadcast_to(x[None], (n,) + x.shape)
    got = lax.all_to_all(slots, axis, 0, 0)
    return got.reshape((n * x.shape[0],) + x.shape[1:])


def tree_gather(x, axis):
    n = lax.axis_size(axis)
    me = lax.axis_index(axis)
    bits = []
    b = n // 2
    while b >= 1:
        bits.append(b)
        b //= 2
    held = x[None]
    for b in bits:
        held = jnp.concatenate([held, lax.ppermute(held, axis, [(i, i ^ b) for i in range(n)])])
    rel = me ^ jnp.arange(n)
    slot = sum(((rel // b) % 2) << j for j, b in enumerate(bits))
    return jnp.take(held, slot, axis=0).reshape((n * x.shape[0],) + x.shape[1:])


def shards(counts, theta, phi, affinity):
    nr, nc = lax.axis_size(ROW), lax.axis_size("col")
    assert nr & (nr - 1) == 0
    nodes = theta.shape[0] * nr * nc
    inverse = 1.0 / nodes
    k = theta.shape[1]
    c = lax.axis_index("col")
    r = lax.axis_index(ROW)
    if nc == 2:
        other = lax.ppermute(theta, "col", SWAP)
        theta_rows = jnp.where(c == 0, jnp.concatenate([theta, other]), jnp.concatenate([other, theta]))
    else:
        theta_rows = gather_rows(theta, "col")
    nchip = lax.axis_size("chip")
    core = lax.axis_index("core")
    by_chip = lax.all_to_all(jnp.broadcast_to(phi[None], (nchip,) + phi.shape), "chip", 0, 0)
    other = lax.ppermute(by_chip, "core", SWAP)
    mr = phi.shape[0]
    special = nc == 2 and nr == 16
    if special:
        def xz(a):
            return jnp.swapaxes(a.reshape(4, 2, mr, k), 0, 1).reshape(8 * mr, k)
        members = jnp.where(core == 0, jnp.concatenate([xz(by_chip), xz(other)]),
                            jnp.concatenate([xz(other), xz(by_chip)]))
        rows = counts.shape[0]
        counts = jnp.transpose(counts.reshape(rows, 4, 2, 2, mr), (0, 3, 2, 1, 4)).reshape(rows, 16 * mr)
    else:
        pair = jnp.where(core == 0, jnp.stack([by_chip, other], axis=1), jnp.stack([other, by_chip], axis=1))
        members = pair.reshape(nr * phi.shape[0], k)
    theta_wide = theta_rows.astype(jnp.float32)
    row_factor = jnp.dot(theta_wide, affinity, precision=HI)
    factor_half = row_factor.astype(jnp.bfloat16)
    rate = jnp.dot(row_factor, members.astype(jnp.float32).T, precision=HI)
    ratio = (1.0 - counts.astype(jnp.float32) / rate).astype(jnp.bfloat16)
    gphi = jnp.dot(ratio, members, preferred_element_type=jnp.float32)
    gcol = lax.dot_general(ratio, factor_half, (((0,), (0,)), ((), ())), preferred_element_type=jnp.float32)
    part = lax.dot_general(gphi, theta_wide, (((0,), (0,)), ((), ())), precision=HI)
    mc = gphi.shape[0] // nc
    deferred = nc == 2 and nr >= 8
    if deferred:
        part_sum = part
    elif nc == 2:
        send = jnp.concatenate([lax.dynamic_slice_in_dim(gphi, (1 - c) * mc, mc), part])
        got = lax.ppermute(send, "col", SWAP)
        gphi_sum = lax.dynamic_slice_in_dim(gphi, c * mc, mc) + got[:mc]
        part_sum = part + got[mc:]
    else:
        slots = jnp.concatenate([gphi.reshape(nc, mc, k), jnp.broadcast_to(part[None], (nc, k, k))], axis=1)
        got = lax.all_to_all(slots, "col", 0, 0)
        gphi_sum = jnp.sum(got[:, :mc], axis=0)
        part_sum = jnp.sum(got[:, mc:], axis=0)
    mr = gcol.shape[0] // nr
    acc = gcol.reshape(nr, mr, k)
    b = 1
    if special:
        half = 8 * mr
        got = lax.ppermute(jnp.concatenate([lax.dynamic_slice_in_dim(gcol, (1 - core) * half, half), part_sum]),
                           ROW, [(i, i ^ 1) for i in range(nr)])
        acc = lax.dynamic_slice_in_dim(gcol, core * half, half) + got[:half]
        part_sum = part_sum + got[half:]
        x = (r // 2) % 2
        half = 4 * mr
        got = lax.ppermute(jnp.concatenate([lax.dynamic_slice_in_dim(acc, (1 - x) * half, half), part_sum]),
                           ROW, [(i, i ^ 2) for i in range(nr)])
        send = jnp.concatenate([lax.dynamic_slice_in_dim(gphi, (1 - c) * mc, mc), part_sum])
        got_col = lax.ppermute(send, "col", SWAP)
        got_diag = lax.ppermute(part_sum, ROW + ("col",), [(i, i ^ 5) for i in range(nr * nc)])
        gphi_sum = lax.dynamic_slice_in_dim(gphi, c * mc, mc) + got_col[:mc]
        acc = (lax.dynamic_slice_in_dim(acc, x * half, half) + got[:half]).reshape(4, mr, k)
        part_sum = (part_sum + got_col[mc:]) + (got[half:] + got_diag)
        b = 4
        deferred = False
    while b < nr // 4:
        pairs = acc.reshape(acc.shape[0] // 2, 2, mr, k)
        mine = (r // b) % 2
        keep = jnp.take(pairs, mine, axis=1)
        away = jnp.take(pairs, 1 - mine, axis=1)
        send = jnp.concatenate([away.reshape(-1, k), part_sum])
        got = lax.ppermute(send, ROW, [(i, i ^ b) for i in range(nr)])
        acc = keep + got[: keep.shape[0] * mr].reshape(keep.shape)
        if deferred and b == 2:
            send = jnp.concatenate([lax.dynamic_slice_in_dim(gphi, (1 - c) * mc, mc), part_sum])
            got_col = lax.ppermute(send, "col", SWAP)
            got_diag = lax.ppermute(part_sum, ROW + ("col",), [(i, i ^ (2 * b + 1)) for i in range(nr * nc)])
            gphi_sum = lax.dynamic_slice_in_dim(gphi, c * mc, mc) + got_col[:mc]
            part_sum = (part_sum + got_col[mc:]) + (got[keep.shape[0] * mr:] + got_diag)
            deferred = False
        else:
            part_sum = part_sum + got[keep.shape[0] * mr:]
        b *= 2
    if acc.shape[0] == 4:
        quad = (r // b) % 4
        held = [part_sum]
        total = jnp.take(acc, quad, axis=0)
        for s in (1, 2, 3):
            send = jnp.concatenate([jnp.take(acc, quad ^ s, axis=0), part_sum])
            got = lax.ppermute(send, ROW, [(i, i ^ (s * b)) for i in range(nr)])
            total = total + got[:mr]
            held.append(got[mr:])
        part_sum = (held[0] + held[1]) + (held[2] + held[3])
        acc = total[None]
    elif acc.shape[0] == 2:
        mine = (r // b) % 2
        send = jnp.concatenate([jnp.take(acc, 1 - mine, axis=0), part_sum])
        got = lax.ppermute(send, ROW, [(i, i ^ b) for i in range(nr)])
        acc = (jnp.take(acc, mine, axis=0) + got[:mr])[None]
        part_sum = part_sum + got[mr:]
    phi_sum = acc[0]
    theta_grad = inverse * jnp.dot(gphi_sum, affinity.T, precision=HI)
    phi_grad = inverse * phi_sum
    affinity_grad = inverse * inverse * part_sum.T
    return (theta_grad, phi_grad, affinity_grad)


def solution(mesh):
    rows, cols = mesh.devices.shape
    split = Mesh(mesh.devices.reshape(rows // 2, 2, cols), ("chip", "core", "col"))
    placed = (P(ROW, "col"), P(ROW + ("col",), None), P(("col",) + ROW, None), P())
    return jax.shard_map(
        shards,
        mesh=split,
        in_specs=placed,
        out_specs=(P(ROW + ("col",), None), P(("col",) + ROW, None), P()),
        check_vma=False,
    )
```
